512 devices in a mesh: diag: 64 (over z_lo, y, x), off: 8 (over z_hi, core).
Axes of the slice: x: 4, y: 8, z: 8 (z_hi: 4, z_lo: 2; z = z_hi * 2 + z_lo), core: 2. Of those that a mesh axis runs over, the one named last changes fastest.
Arguments:
- trunk: bfloat16 [64, 1, 64, 128], P('diag'), may hold values from -6 to 6
- w_first: bfloat16 [48, 128, 3, 3], replicated, may hold values from -0.1875 to 0.1875
- b_first: float32 [48], replicated, may hold values from -3 to 3
- w_second: bfloat16 [48, 48, 3, 3], replicated, may hold values from -0.3125 to 0.3125
- b_second: float32 [48], replicated, may hold values from -3 to 3
Outputs:
- contact_tiles: bfloat16 [64, 8, 1, 48, 128, 128], P('diag', 'off')
The draws below stay inside these ranges and needn't reach their ends.
All inputs are finite; a program needn't handle non-finite values.
Results may differ from the reference program's by a relative error of at most 0.0043.
Values may be sent and summed in bfloat16 or wider, within the bound.
No kernel may reach another device: no remote copies, remote signals or barrier semaphores. Data moves between devices by JAX's collectives and lax.ppermute only.
A program may use at most 128 MiB of HBM per device.

```python
import jax
import jax.numpy as jnp
from jax import lax

W = 128
C = 64
HID = 48
B = 1
NP = 64
BAND = 8
NB = 8192


def steps_of(key, dims, pieces, low, largest):
    def one(axis_at, parts):
        heights = jax.random.uniform(jax.random.fold_in(jax.random.fold_in(key, 6), axis_at), (parts,), jnp.float32, low / len(pieces), largest / len(pieces))
        return jnp.repeat(jnp.exp(heights), dims[axis_at] // parts).reshape((-1,) + (1,) * (len(dims) - axis_at - 1))

    loudness = one(*pieces[0])
    for cut in pieces[1:]:
        loudness = loudness * one(*cut)
    return loudness


def normal_values(key, dims, scale, reach, split=(), kind=jnp.bfloat16):
    gain = steps_of(key, dims, split, -0.22, 0.18) if split else 1.0
    entries = jax.random.normal(key, dims, jnp.float32) * scale * gain
    return jnp.minimum(jnp.maximum(entries, -reach), reach).astype(kind)


def setup_inputs(seed: int = 0) -> dict:
    splits = jax.random.split(jax.random.key(seed), 6)
    return {
        "trunk": normal_values(splits[0], (NP, B, C, W), 1.0, 6.0, ((0, 64),)),
        "w_first": normal_values(splits[1], (HID, 2 * C, 3, 3), (18 * C) ** -0.5, 0.1875),
        "b_first": normal_values(splits[2], (HID,), 0.5, 3.0, (), jnp.float32),
        "w_second": normal_values(splits[3], (HID, HID, 3, 3), (9 * HID) ** -0.5, 0.3125),
        "b_second": normal_values(splits[4], (HID,), 0.5, 3.0, (), jnp.float32),
    }


def band_mask(row_tile, col_tile, start, extent):
    offsets = start + jnp.arange(extent, dtype=jnp.int32)
    row_bins = row_tile * W + offsets
    col_bins = col_tile * W + offsets
    row_ok = (row_bins >= 0) & (row_bins < NB)
    col_ok = (col_bins >= 0) & (col_bins < NB)
    gap = jnp.floor_divide(col_bins, W)[None, :] - jnp.floor_divide(row_bins, W)[:, None]
    return row_ok[:, None] & col_ok[None, :] & (gap >= 0) & (gap < BAND)


def dilated(inputs, weights, rate):
    return lax.conv_general_dilated(inputs, weights, (1, 1), "VALID", rhs_dilation=(rate, rate),
                                    dimension_numbers=("NCHW", "OIHW", "NCHW"),
                                    precision=lax.Precision.HIGHEST)


def reference(trunk, w_first, b_first, w_second, b_second):
    flat = jnp.transpose(trunk.astype(jnp.float32), (1, 2, 0, 3)).reshape(B, C, NB)
    padded = jnp.pad(flat, ((0, 0), (0, 0), (6, 6 + BAND * W)))
    first = w_first.astype(jnp.float32)
    second = w_second.astype(jnp.float32)
    extent = W + 12

    def one_tile(index):
        row_tile = (index // BAND).astype(jnp.int32)
        col_tile = (row_tile + index % BAND).astype(jnp.int32)
        rows = lax.dynamic_slice(padded, (jnp.int32(0), jnp.int32(0), row_tile * W), (B, C, extent))
        cols = lax.dynamic_slice(padded, (jnp.int32(0), jnp.int32(0), col_tile * W), (B, C, extent))
        features = jnp.concatenate([jnp.broadcast_to(rows[:, :, :, None], (B, C, extent, extent)),
                                    jnp.broadcast_to(cols[:, :, None, :], (B, C, extent, extent))], axis=1)
        features = jnp.where(band_mask(row_tile, col_tile, -6, extent)[None, None], features, 0.0)
        pre = dilated(features, first, 2) + b_first[None, :, None, None]
        hidden = jnp.where(band_mask(row_tile, col_tile, -4, extent - 4)[None, None],
                           jnp.maximum(pre, 0.0), 0.0)
        hidden = hidden.astype(jnp.bfloat16).astype(jnp.float32)
        result = dilated(hidden, second, 4) + b_second[None, :, None, None]
        return result.astype(jnp.bfloat16)

    tiles = lax.map(one_tile, jnp.arange(NP * BAND, dtype=jnp.int32))
    return tiles.reshape(NP, BAND, B, HID, W, W)
```

```python
import jax
import jax.numpy as jnp
from jax import lax
from jax.sharding import PartitionSpec as P


def band_mask(row_tile, col_tile, start, extent, width, nbins, offsets_total):
    offsets = start + jnp.arange(extent, dtype=jnp.int32)
    row_bins = row_tile * width + offsets
    col_bins = col_tile * width + offsets
    row_ok = (row_bins >= 0) & (row_bins < nbins)
    col_ok = (col_bins >= 0) & (col_bins < nbins)
    gap = jnp.floor_divide(col_bins, width)[None, :] - jnp.floor_divide(row_bins, width)[:, None]
    return row_ok[:, None] & col_ok[None, :] & (gap >= 0) & (gap < offsets_total)


def fetch(trunk, shift_of, n_diag, n_off, offset):
    pairs = []
    for d in range(n_diag):
        for o in range(n_off):
            src = d + shift_of(o)
            if 0 <= src < n_diag and src != d:
                pairs.append((src * n_off + o, d * n_off + o))
    moved = lax.ppermute(trunk, ("diag", "off"), pairs)
    selves = [o for o in range(n_off) if shift_of(o) == 0]
    if not selves:
        return moved
    is_self = jnp.zeros((), jnp.bool_)
    for o in selves:
        is_self = is_self | (offset == o)
    return jnp.where(is_self, trunk, moved)


def local(trunk, w_first, b_first, w_second, b_second):
    samples = trunk.shape[1]
    channels = trunk.shape[2]
    width = trunk.shape[3]
    hidden_width = w_first.shape[0]
    n_off = lax.axis_size("off")
    n_diag = lax.axis_size("diag")
    nbins = n_diag * width
    row_tile = lax.axis_index("diag")
    offset = lax.axis_index("off")
    col_tile = row_tile + offset

    row_prev = fetch(trunk, lambda o: -1, n_diag, n_off, offset)
    row_next = fetch(trunk, lambda o: 1, n_diag, n_off, offset)
    col_prev = fetch(trunk, lambda o: o - 1, n_diag, n_off, offset)
    col_here = fetch(trunk, lambda o: o, n_diag, n_off, offset)
    col_next = fetch(trunk, lambda o: o + 1, n_diag, n_off, offset)

    row_line = jnp.concatenate([row_prev[0], trunk[0], row_next[0]], axis=-1)
    col_line = jnp.concatenate([col_prev[0], col_here[0], col_next[0]], axis=-1)

    extent = width + 12
    inner_size = width + 8
    rows = row_line[:, :, width - 6 : width - 6 + extent]
    cols = col_line[:, :, width - 6 : width - 6 + extent]
    outer_mask = band_mask(row_tile, col_tile, -6, extent, width, nbins, n_off)
    features = jnp.concatenate(
        [
            jnp.broadcast_to(rows[:, :, :, None], (samples, channels, extent, extent)),
            jnp.broadcast_to(cols[:, :, None, :], (samples, channels, extent, extent)),
        ],
        axis=1,
    )
    features = jnp.where(outer_mask[None, None], features, jnp.zeros_like(features))
    pre = jnp.zeros((samples, hidden_width, inner_size, inner_size), jnp.float32)
    for tap_row in range(3):
        for tap_col in range(3):
            window_cells = features[
                :, :, 2 * tap_row : 2 * tap_row + inner_size, 2 * tap_col : 2 * tap_col + inner_size
            ]
            pre = pre + jnp.einsum(
                "hc,bcij->bhij",
                w_first[:, :, tap_row, tap_col],
                window_cells,
                preferred_element_type=jnp.float32,
            )
    inner_mask = band_mask(row_tile, col_tile, -4, inner_size, width, nbins, n_off)
    hidden = jnp.where(
        inner_mask[None, None], jnp.maximum(pre + b_first[None, :, None, None], 0.0), 0.0
    )
    hidden = hidden.astype(jnp.bfloat16)
    result = jnp.zeros((samples, hidden_width, width, width), jnp.float32)
    for tap_row in range(3):
        for tap_col in range(3):
            window_cells = hidden[
                :, :, 4 * tap_row : 4 * tap_row + width, 4 * tap_col : 4 * tap_col + width
            ]
            result = result + jnp.einsum(
                "hk,bkij->bhij",
                w_second[:, :, tap_row, tap_col],
                window_cells,
                preferred_element_type=jnp.float32,
            )
    result = (result + b_second[None, :, None, None]).astype(jnp.bfloat16)
    return result[None, None]


def solution(mesh):
    placed = (P("diag", None, None, None), P(), P(), P(), P())
    return jax.shard_map(
        local,
        mesh=mesh,
        in_specs=placed,
        out_specs=P("diag", "off", None, None, None, None),
        check_vma=False,
    )
```

```python
import jax
import jax.numpy as jnp
from jax import lax
from jax.sharding import PartitionSpec as P


def band_mask(row_tile, col_tile, start, extent, width, nbins, offsets_total):
    offsets = start + jnp.arange(extent, dtype=jnp.int32)
    row_bins = row_tile * width + offsets
    col_bins = col_tile * width + offsets
    row_ok = (row_bins >= 0) & (row_bins < nbins)
    col_ok = (col_bins >= 0) & (col_bins < nbins)
    gap = jnp.floor_divide(col_bins, width)[None, :] - jnp.floor_divide(row_bins, width)[:, None]
    return row_ok[:, None] & col_ok[None, :] & (gap >= 0) & (gap < offsets_total)


def fetch(trunk, shift_of, n_diag, n_off, offset):
    pairs = []
    for d in range(n_diag):
        for o in range(n_off):
            src = d + shift_of(o)
            if 0 <= src < n_diag and src != d:
                pairs.append((src * n_off + o, d * n_off + o))
    moved = lax.ppermute(trunk, ("diag", "off"), pairs)
    selves = [o for o in range(n_off) if shift_of(o) == 0]
    if not selves:
        return moved
    is_self = jnp.zeros((), jnp.bool_)
    for o in selves:
        is_self = is_self | (offset == o)
    return jnp.where(is_self, trunk, moved)


def block_indicator(tile, start, extent, width, nbins):
    bins = tile * width + start + jnp.arange(extent, dtype=jnp.int32)
    ok = (bins >= 0) & (bins < nbins)
    block = jnp.floor_divide(bins, width) - tile + 1
    return (ok[None, :] & (block[None, :] == jnp.arange(3, dtype=jnp.int32)[:, None])).astype(jnp.float32)


def split_bf16(value):
    high = value.astype(jnp.bfloat16)
    low = (value - high.astype(jnp.float32)).astype(jnp.bfloat16)
    return high, low


def first_conv(rows, cols, w_first, row_tile, col_tile, offset, width, nbins, n_off):
    channels = rows.shape[0]
    extent = rows.shape[1]
    size = extent - 4
    a_ind = block_indicator(row_tile, -6, extent, width, nbins)
    b_ind = block_indicator(col_tile, -6, extent, width, nbins)
    steps = jnp.arange(3, dtype=jnp.int32)
    gap = offset + steps[None, :] - steps[:, None]
    g = ((gap >= 0) & (gap < n_off)).astype(jnp.float32)
    r = jnp.einsum("hcuv,ci->uvhi", w_first[:, :channels], rows, preferred_element_type=jnp.float32)
    c = jnp.einsum("hcuv,cj->uvhj", w_first[:, channels:], cols, preferred_element_type=jnp.float32)
    p_row = sum(
        a_ind[None, None, :, 2 * u : 2 * u + size] * r[u][:, :, None, 2 * u : 2 * u + size]
        for u in range(3)
    )
    b_sel = jnp.einsum("ab,bj->aj", g, b_ind)
    q_col = jnp.stack([b_sel[:, 2 * v : 2 * v + size] for v in range(3)], axis=1)
    p_col = sum(
        b_ind[None, None, :, 2 * v : 2 * v + size] * c[:, v][:, :, None, 2 * v : 2 * v + size]
        for v in range(3)
    )
    a_sel = jnp.einsum("ab,ai->bi", g, a_ind)
    q_row = jnp.stack([a_sel[:, 2 * u : 2 * u + size] for u in range(3)], axis=1)
    p_row_hi, p_row_lo = split_bf16(p_row)
    p_col_hi, p_col_lo = split_bf16(p_col)
    q_col = q_col.astype(jnp.bfloat16)
    q_row = q_row.astype(jnp.bfloat16)
    term_row = jnp.einsum("vhai,avj->hij", p_row_hi, q_col, preferred_element_type=jnp.float32)
    term_row = term_row + jnp.einsum("vhai,avj->hij", p_row_lo, q_col, preferred_element_type=jnp.float32)
    term_col = jnp.einsum("bui,uhbj->hij", q_row, p_col_hi, preferred_element_type=jnp.float32)
    term_col = term_col + jnp.einsum("bui,uhbj->hij", q_row, p_col_lo, preferred_element_type=jnp.float32)
    return term_row + term_col


def local(trunk, w_first, b_first, w_second, b_second):
    samples = trunk.shape[1]
    channels = trunk.shape[2]
    width = trunk.shape[3]
    hidden_width = w_first.shape[0]
    n_off = lax.axis_size("off")
    n_diag = lax.axis_size("diag")
    nbins = n_diag * width
    row_tile = lax.axis_index("diag")
    offset = lax.axis_index("off")
    col_tile = row_tile + offset

    row_prev = fetch(trunk, lambda o: -1, n_diag, n_off, offset)
    row_next = fetch(trunk, lambda o: 1, n_diag, n_off, offset)
    col_prev = fetch(trunk, lambda o: o - 1, n_diag, n_off, offset)
    col_here = fetch(trunk, lambda o: o, n_diag, n_off, offset)
    col_next = fetch(trunk, lambda o: o + 1, n_diag, n_off, offset)

    row_line = jnp.concatenate([row_prev[0], trunk[0], row_next[0]], axis=-1)
    col_line = jnp.concatenate([col_prev[0], col_here[0], col_next[0]], axis=-1)

    extent = width + 12
    inner_size = width + 8
    rows = row_line[:, :, width - 6 : width - 6 + extent]
    cols = col_line[:, :, width - 6 : width - 6 + extent]
    pre = first_conv(rows[0], cols[0], w_first, row_tile, col_tile, offset, width, nbins, n_off)
    pre = pre[None]
    inner_mask = band_mask(row_tile, col_tile, -4, inner_size, width, nbins, n_off)
    hidden = jnp.where(
        inner_mask[None, None], jnp.maximum(pre + b_first[None, :, None, None], 0.0), 0.0
    )
    hidden = hidden.astype(jnp.bfloat16)
    result = jnp.zeros((samples, hidden_width, width, width), jnp.float32)
    for tap_row in range(3):
        for tap_col in range(3):
            window_cells = hidden[
                :, :, 4 * tap_row : 4 * tap_row + width, 4 * tap_col : 4 * tap_col + width
            ]
            result = result + jnp.einsum(
                "hk,bkij->bhij",
                w_second[:, :, tap_row, tap_col],
                window_cells,
                preferred_element_type=jnp.float32,
            )
    result = (result + b_second[None, :, None, None]).astype(jnp.bfloat16)
    return result[None, None]


def solution(mesh):
    placed = (P("diag", None, None, None), P(), P(), P(), P())
    return jax.shard_map(
        local,
        mesh=mesh,
        in_specs=placed,
        out_specs=P("diag", "off", None, None, None, None),
        check_vma=False,
    )
```

```python
import jax
import jax.numpy as jnp
from jax import lax
from jax.sharding import PartitionSpec as P


def band_mask(row_tile, col_tile, start, extent, width, nbins, offsets_total):
    offsets = start + jnp.arange(extent, dtype=jnp.int32)
    row_bins = row_tile * width + offsets
    col_bins = col_tile * width + offsets
    row_ok = (row_bins >= 0) & (row_bins < nbins)
    col_ok = (col_bins >= 0) & (col_bins < nbins)
    gap = jnp.floor_divide(col_bins, width)[None, :] - jnp.floor_divide(row_bins, width)[:, None]
    return row_ok[:, None] & col_ok[None, :] & (gap >= 0) & (gap < offsets_total)


def fetch(trunk, shift_of, n_diag, n_off, offset):
    pairs = []
    for d in range(n_diag):
        for o in range(n_off):
            src = d + shift_of(o)
            if 0 <= src < n_diag and src != d:
                pairs.append((src * n_off + o, d * n_off + o))
    moved = lax.ppermute(trunk, ("diag", "off"), pairs)
    selves = [o for o in range(n_off) if shift_of(o) == 0]
    if not selves:
        return moved
    is_self = jnp.zeros((), jnp.bool_)
    for o in selves:
        is_self = is_self | (offset == o)
    return jnp.where(is_self, trunk, moved)


def block_indicator(tile, start, extent, width, nbins):
    bins = tile * width + start + jnp.arange(extent, dtype=jnp.int32)
    ok = (bins >= 0) & (bins < nbins)
    block = jnp.floor_divide(bins, width) - tile + 1
    return (ok[None, :] & (block[None, :] == jnp.arange(3, dtype=jnp.int32)[:, None])).astype(jnp.float32)


def split_bf16(value):
    high = lax.reduce_precision(value, exponent_bits=8, mantissa_bits=7)
    low = value - high
    return high.astype(jnp.bfloat16), low.astype(jnp.bfloat16)


def first_conv(rows, cols, w_first, row_tile, col_tile, offset, width, nbins, n_off):
    channels = rows.shape[0]
    extent = rows.shape[1]
    size = extent - 4
    a_ind = block_indicator(row_tile, -6, extent, width, nbins)
    b_ind = block_indicator(col_tile, -6, extent, width, nbins)
    steps = jnp.arange(3, dtype=jnp.int32)
    gap = offset + steps[None, :] - steps[:, None]
    g = ((gap >= 0) & (gap < n_off)).astype(jnp.float32)
    r = jnp.einsum("hcuv,ci->uvhi", w_first[:, :channels], rows, preferred_element_type=jnp.float32)
    c = jnp.einsum("hcuv,cj->uvhj", w_first[:, channels:], cols, preferred_element_type=jnp.float32)
    p_row = sum(
        a_ind[None, None, :, 2 * u : 2 * u + size] * r[u][:, :, None, 2 * u : 2 * u + size]
        for u in range(3)
    )
    b_sel = jnp.einsum("ab,bj->aj", g, b_ind)
    q_col = jnp.stack([b_sel[:, 2 * v : 2 * v + size] for v in range(3)], axis=1)
    p_col = sum(
        b_ind[None, None, :, 2 * v : 2 * v + size] * c[:, v][:, :, None, 2 * v : 2 * v + size]
        for v in range(3)
    )
    a_sel = jnp.einsum("ab,ai->bi", g, a_ind)
    q_row = jnp.stack([a_sel[:, 2 * u : 2 * u + size] for u in range(3)], axis=1)
    p_row_hi, p_row_lo = split_bf16(p_row)
    p_col_hi, p_col_lo = split_bf16(p_col)
    q_col = q_col.astype(jnp.bfloat16)
    q_row = q_row.astype(jnp.bfloat16)
    term_row = jnp.einsum("vhai,avj->hij", p_row_hi, q_col, preferred_element_type=jnp.float32)
    term_row = term_row + jnp.einsum("vhai,avj->hij", p_row_lo, q_col, preferred_element_type=jnp.float32)
    term_col = jnp.einsum("bui,uhbj->hij", q_row, p_col_hi, preferred_element_type=jnp.float32)
    term_col = term_col + jnp.einsum("bui,uhbj->hij", q_row, p_col_lo, preferred_element_type=jnp.float32)
    return term_row + term_col


def local(trunk, w_first, b_first, w_second, b_second):
    samples = trunk.shape[1]
    channels = trunk.shape[2]
    width = trunk.shape[3]
    hidden_width = w_first.shape[0]
    n_off = lax.axis_size("off")
    n_diag = lax.axis_size("diag")
    nbins = n_diag * width
    row_tile = lax.axis_index("diag")
    offset = lax.axis_index("off")
    col_tile = row_tile + offset

    row_prev = fetch(trunk, lambda o: -1, n_diag, n_off, offset)
    row_next = fetch(trunk, lambda o: 1, n_diag, n_off, offset)
    col_prev = fetch(trunk, lambda o: o - 1, n_diag, n_off, offset)
    col_here = fetch(trunk, lambda o: o, n_diag, n_off, offset)
    col_next = fetch(trunk, lambda o: o + 1, n_diag, n_off, offset)

    row_line = jnp.concatenate([row_prev[0], trunk[0], row_next[0]], axis=-1)
    col_line = jnp.concatenate([col_prev[0], col_here[0], col_next[0]], axis=-1)

    extent = width + 12
    inner_size = width + 8
    rows = row_line[:, :, width - 6 : width - 6 + extent]
    cols = col_line[:, :, width - 6 : width - 6 + extent]
    pre = first_conv(rows[0], cols[0], w_first, row_tile, col_tile, offset, width, nbins, n_off)
    pre = pre[None]
    inner_mask = band_mask(row_tile, col_tile, -4, inner_size, width, nbins, n_off)
    hidden = jnp.where(
        inner_mask[None, None], jnp.maximum(pre + b_first[None, :, None, None], 0.0), 0.0
    )
    hidden = hidden.astype(jnp.bfloat16)
    result = jnp.zeros((samples, hidden_width, width, width), jnp.float32)
    for tap_row in range(3):
        for tap_col in range(3):
            window_cells = hidden[
                :, :, 4 * tap_row : 4 * tap_row + width, 4 * tap_col : 4 * tap_col + width
            ]
            result = result + jnp.einsum(
                "hk,bkij->bhij",
                w_second[:, :, tap_row, tap_col],
                window_cells,
                preferred_element_type=jnp.float32,
            )
    result = (result + b_second[None, :, None, None]).astype(jnp.bfloat16)
    return result[None, None]


def solution(mesh):
    placed = (P("diag", None, None, None), P(), P(), P(), P())
    return jax.shard_map(
        local,
        mesh=mesh,
        in_specs=placed,
        out_specs=P("diag", "off", None, None, None, None),
        check_vma=False,
    )
```

```python
import jax
import jax.numpy as jnp
from jax import lax
from jax.sharding import PartitionSpec as P
from jax.experimental import pallas as pl


def band_mask(row_tile, col_tile, start, extent, width, nbins, offsets_total):
    offsets = start + jnp.arange(extent, dtype=jnp.int32)
    row_bins = row_tile * width + offsets
    col_bins = col_tile * width + offsets
    row_ok = (row_bins >= 0) & (row_bins < nbins)
    col_ok = (col_bins >= 0) & (col_bins < nbins)
    gap = jnp.floor_divide(col_bins, width)[None, :] - jnp.floor_divide(row_bins, width)[:, None]
    return row_ok[:, None] & col_ok[None, :] & (gap >= 0) & (gap < offsets_total)


def fetch(trunk, shift_of, n_diag, n_off, offset):
    pairs = []
    for d in range(n_diag):
        for o in range(n_off):
            src = d + shift_of(o)
            if 0 <= src < n_diag and src != d:
                pairs.append((src * n_off + o, d * n_off + o))
    moved = lax.ppermute(trunk, ("diag", "off"), pairs)
    selves = [o for o in range(n_off) if shift_of(o) == 0]
    if not selves:
        return moved
    is_self = jnp.zeros((), jnp.bool_)
    for o in selves:
        is_self = is_self | (offset == o)
    return jnp.where(is_self, trunk, moved)


def block_indicator(tile, start, extent, width, nbins):
    bins = tile * width + start + jnp.arange(extent, dtype=jnp.int32)
    ok = (bins >= 0) & (bins < nbins)
    block = jnp.floor_divide(bins, width) - tile + 1
    return (ok[None, :] & (block[None, :] == jnp.arange(3, dtype=jnp.int32)[:, None])).astype(jnp.float32)


def split_bf16(value):
    high = lax.reduce_precision(value, exponent_bits=8, mantissa_bits=7)
    low = value - high
    return high.astype(jnp.bfloat16), low.astype(jnp.bfloat16)


def first_conv(rows, cols, w_first, row_tile, col_tile, offset, width, nbins, n_off):
    channels = rows.shape[0]
    extent = rows.shape[1]
    size = extent - 4
    a_ind = block_indicator(row_tile, -6, extent, width, nbins)
    b_ind = block_indicator(col_tile, -6, extent, width, nbins)
    steps = jnp.arange(3, dtype=jnp.int32)
    gap = offset + steps[None, :] - steps[:, None]
    g = ((gap >= 0) & (gap < n_off)).astype(jnp.float32)
    r = jnp.einsum("hcuv,ci->uvhi", w_first[:, :channels], rows, preferred_element_type=jnp.float32)
    c = jnp.einsum("hcuv,cj->uvhj", w_first[:, channels:], cols, preferred_element_type=jnp.float32)
    p_row = sum(
        a_ind[None, None, :, 2 * u : 2 * u + size] * r[u][:, :, None, 2 * u : 2 * u + size]
        for u in range(3)
    )
    b_sel = jnp.einsum("ab,bj->aj", g, b_ind)
    q_col = jnp.stack([b_sel[:, 2 * v : 2 * v + size] for v in range(3)], axis=1)
    p_col = sum(
        b_ind[None, None, :, 2 * v : 2 * v + size] * c[:, v][:, :, None, 2 * v : 2 * v + size]
        for v in range(3)
    )
    a_sel = jnp.einsum("ab,ai->bi", g, a_ind)
    q_row = jnp.stack([a_sel[:, 2 * u : 2 * u + size] for u in range(3)], axis=1)
    p_row_hi, p_row_lo = split_bf16(p_row)
    p_col_hi, p_col_lo = split_bf16(p_col)
    q_col = q_col.astype(jnp.bfloat16)
    q_row = q_row.astype(jnp.bfloat16)
    term_row = jnp.einsum("vhai,avj->ihj", p_row_hi, q_col, preferred_element_type=jnp.float32)
    term_row = term_row + jnp.einsum("vhai,avj->ihj", p_row_lo, q_col, preferred_element_type=jnp.float32)
    term_col = jnp.einsum("bui,uhbj->ihj", q_row, p_col_hi, preferred_element_type=jnp.float32)
    term_col = term_col + jnp.einsum("bui,uhbj->ihj", q_row, p_col_lo, preferred_element_type=jnp.float32)
    return term_row + term_col


ROWS_PER_STEP = 8


def second_conv_kernel(w_ref, b_ref, hidden_ref, out_ref):
    step = pl.program_id(0)
    width = out_ref.shape[2]
    for r in range(ROWS_PER_STEP):
        i = step * ROWS_PER_STEP + r
        acc = None
        for u in range(3):
            row = hidden_ref[i + 4 * u]
            for v in range(3):
                part = jnp.dot(w_ref[3 * u + v], row[:, 4 * v : 4 * v + width],
                               preferred_element_type=jnp.float32)
                acc = part if acc is None else acc + part
        out_ref[:, r, :] = (acc + b_ref[...]).astype(out_ref.dtype)


def second_conv(hidden, w_second, b_second):
    rows_in, hid, cols_in = hidden.shape
    width = rows_in - 8
    taps = jnp.transpose(w_second, (2, 3, 0, 1)).reshape(9, hid, hid)
    return pl.pallas_call(
        second_conv_kernel,
        grid=(width // ROWS_PER_STEP,),
        in_specs=[
            pl.BlockSpec((9, hid, hid), lambda s: (0, 0, 0)),
            pl.BlockSpec((hid, 1), lambda s: (0, 0)),
            pl.BlockSpec((rows_in, hid, cols_in), lambda s: (0, 0, 0)),
        ],
        out_specs=pl.BlockSpec((hid, ROWS_PER_STEP, width), lambda s: (0, s, 0)),
        out_shape=jax.ShapeDtypeStruct((hid, width, width), jnp.bfloat16),
    )(taps, b_second.reshape(hid, 1), hidden)


def local(trunk, w_first, b_first, w_second, b_second):
    samples = trunk.shape[1]
    channels = trunk.shape[2]
    width = trunk.shape[3]
    hidden_width = w_first.shape[0]
    n_off = lax.axis_size("off")
    n_diag = lax.axis_size("diag")
    nbins = n_diag * width
    row_tile = lax.axis_index("diag")
    offset = lax.axis_index("off")
    col_tile = row_tile + offset

    row_prev = fetch(trunk, lambda o: -1, n_diag, n_off, offset)
    row_next = fetch(trunk, lambda o: 1, n_diag, n_off, offset)
    col_prev = fetch(trunk, lambda o: o - 1, n_diag, n_off, offset)
    col_here = fetch(trunk, lambda o: o, n_diag, n_off, offset)
    col_next = fetch(trunk, lambda o: o + 1, n_diag, n_off, offset)

    row_line = jnp.concatenate([row_prev[0], trunk[0], row_next[0]], axis=-1)
    col_line = jnp.concatenate([col_prev[0], col_here[0], col_next[0]], axis=-1)

    extent = width + 12
    inner_size = width + 8
    rows = row_line[:, :, width - 6 : width - 6 + extent]
    cols = col_line[:, :, width - 6 : width - 6 + extent]
    pre = first_conv(rows[0], cols[0], w_first, row_tile, col_tile, offset, width, nbins, n_off)
    inner_mask = band_mask(row_tile, col_tile, -4, inner_size, width, nbins, n_off)
    hidden = jnp.where(
        inner_mask[:, None, :], jnp.maximum(pre + b_first[None, :, None], 0.0), 0.0
    )
    hidden = hidden.astype(jnp.bfloat16)
    result = second_conv(hidden, w_second, b_second)
    return result[None, None, None]


def solution(mesh):
    placed = (P("diag", None, None, None), P(), P(), P(), P())
    return jax.shard_map(
        local,
        mesh=mesh,
        in_specs=placed,
        out_specs=P("diag", "off", None, None, None, None),
        check_vma=False,
    )
```

```python
import jax
import jax.numpy as jnp
from jax import lax
from jax.sharding import PartitionSpec as P
from jax.experimental import pallas as pl


def band_mask(row_tile, col_tile, start, extent, width, nbins, offsets_total):
    offsets = start + jnp.arange(extent, dtype=jnp.int32)
    row_bins = row_tile * width + offsets
    col_bins = col_tile * width + offsets
    row_ok = (row_bins >= 0) & (row_bins < nbins)
    col_ok = (col_bins >= 0) & (col_bins < nbins)
    gap = jnp.floor_divide(col_bins, width)[None, :] - jnp.floor_divide(row_bins, width)[:, None]
    return row_ok[:, None] & col_ok[None, :] & (gap >= 0) & (gap < offsets_total)


def fetch(trunk, shift_of, n_diag, n_off, offset):
    pairs = []
    for d in range(n_diag):
        for o in range(n_off):
            src = d + shift_of(o)
            if 0 <= src < n_diag and src != d:
                pairs.append((src * n_off + o, d * n_off + o))
    moved = lax.ppermute(trunk, ("diag", "off"), pairs)
    selves = [o for o in range(n_off) if shift_of(o) == 0]
    if not selves:
        return moved
    is_self = jnp.zeros((), jnp.bool_)
    for o in selves:
        is_self = is_self | (offset == o)
    return jnp.where(is_self, trunk, moved)


def block_indicator(tile, start, extent, width, nbins):
    bins = tile * width + start + jnp.arange(extent, dtype=jnp.int32)
    ok = (bins >= 0) & (bins < nbins)
    block = jnp.floor_divide(bins, width) - tile + 1
    return (ok[None, :] & (block[None, :] == jnp.arange(3, dtype=jnp.int32)[:, None])).astype(jnp.float32)


def split_bf16(value):
    high = lax.reduce_precision(value, exponent_bits=8, mantissa_bits=7)
    low = value - high
    return high.astype(jnp.bfloat16), low.astype(jnp.bfloat16)


def first_conv(rows, cols, w_first, row_tile, col_tile, offset, width, nbins, n_off):
    channels = rows.shape[0]
    extent = rows.shape[1]
    size = extent - 4
    a_ind = block_indicator(row_tile, -6, extent, width, nbins)
    b_ind = block_indicator(col_tile, -6, extent, width, nbins)
    steps = jnp.arange(3, dtype=jnp.int32)
    gap = offset + steps[None, :] - steps[:, None]
    g = ((gap >= 0) & (gap < n_off)).astype(jnp.float32)
    r = jnp.einsum("hcuv,ci->uvhi", w_first[:, :channels], rows, preferred_element_type=jnp.float32)
    c = jnp.einsum("hcuv,cj->uvhj", w_first[:, channels:], cols, preferred_element_type=jnp.float32)
    p_row = sum(
        a_ind[None, None, :, 2 * u : 2 * u + size] * r[u][:, :, None, 2 * u : 2 * u + size]
        for u in range(3)
    )
    b_sel = jnp.einsum("ab,bj->aj", g, b_ind)
    q_col = jnp.stack([b_sel[:, 2 * v : 2 * v + size] for v in range(3)], axis=1)
    p_col = sum(
        b_ind[None, None, :, 2 * v : 2 * v + size] * c[:, v][:, :, None, 2 * v : 2 * v + size]
        for v in range(3)
    )
    a_sel = jnp.einsum("ab,ai->bi", g, a_ind)
    q_row = jnp.stack([a_sel[:, 2 * u : 2 * u + size] for u in range(3)], axis=1)
    taps = 9
    hid = p_row.shape[1]
    p_row = jnp.transpose(p_row, (3, 1, 2, 0)).reshape(size, hid, taps)
    p_col = jnp.transpose(p_col, (2, 0, 1, 3)).reshape(taps, hid, size)
    p_row_hi, p_row_lo = split_bf16(p_row)
    p_col_hi, p_col_lo = split_bf16(p_col)
    q_col = q_col.reshape(taps, size).astype(jnp.bfloat16)
    q_row = jnp.transpose(q_row, (2, 0, 1)).reshape(size, taps).astype(jnp.bfloat16)
    p_row_both = jnp.concatenate([p_row_hi, p_row_lo], axis=2)
    p_col_both = jnp.concatenate([p_col_hi, p_col_lo], axis=0)
    term_row = jnp.einsum("ihk,kj->ihj", p_row_both, jnp.concatenate([q_col, q_col], axis=0),
                          preferred_element_type=jnp.float32)
    term_col = jnp.einsum("ik,khj->ihj", jnp.concatenate([q_row, q_row], axis=1), p_col_both,
                          preferred_element_type=jnp.float32)
    return term_row + term_col


ROWS_PER_STEP = 8


def second_conv_kernel(w_ref, b_ref, hidden_ref, out_ref):
    step = pl.program_id(0)
    width = out_ref.shape[2]
    for r in range(ROWS_PER_STEP):
        i = step * ROWS_PER_STEP + r
        acc = None
        for u in range(3):
            row = hidden_ref[i + 4 * u]
            for v in range(3):
                part = jnp.dot(w_ref[3 * u + v], row[:, 4 * v : 4 * v + width],
                               preferred_element_type=jnp.float32)
                acc = part if acc is None else acc + part
        out_ref[:, r, :] = (acc + b_ref[...]).astype(out_ref.dtype)


def second_conv(hidden, w_second, b_second):
    rows_in, hid, cols_in = hidden.shape
    width = rows_in - 8
    taps = jnp.transpose(w_second, (2, 3, 0, 1)).reshape(9, hid, hid)
    return pl.pallas_call(
        second_conv_kernel,
        grid=(width // ROWS_PER_STEP,),
        in_specs=[
            pl.BlockSpec((9, hid, hid), lambda s: (0, 0, 0)),
            pl.BlockSpec((hid, 1), lambda s: (0, 0)),
            pl.BlockSpec((rows_in, hid, cols_in), lambda s: (0, 0, 0)),
        ],
        out_specs=pl.BlockSpec((hid, ROWS_PER_STEP, width), lambda s: (0, s, 0)),
        out_shape=jax.ShapeDtypeStruct((hid, width, width), jnp.bfloat16),
    )(taps, b_second.reshape(hid, 1), hidden)


def local(trunk, w_first, b_first, w_second, b_second):
    samples = trunk.shape[1]
    channels = trunk.shape[2]
    width = trunk.shape[3]
    hidden_width = w_first.shape[0]
    n_off = lax.axis_size("off")
    n_diag = lax.axis_size("diag")
    nbins = n_diag * width
    row_tile = lax.axis_index("diag")
    offset = lax.axis_index("off")
    col_tile = row_tile + offset

    row_prev = fetch(trunk, lambda o: -1, n_diag, n_off, offset)
    row_next = fetch(trunk, lambda o: 1, n_diag, n_off, offset)
    col_prev = fetch(trunk, lambda o: o - 1, n_diag, n_off, offset)
    col_here = fetch(trunk, lambda o: o, n_diag, n_off, offset)
    col_next = fetch(trunk, lambda o: o + 1, n_diag, n_off, offset)

    row_line = jnp.concatenate([row_prev[0], trunk[0], row_next[0]], axis=-1)
    col_line = jnp.concatenate([col_prev[0], col_here[0], col_next[0]], axis=-1)

    extent = width + 12
    inner_size = width + 8
    rows = row_line[:, :, width - 6 : width - 6 + extent]
    cols = col_line[:, :, width - 6 : width - 6 + extent]
    pre = first_conv(rows[0], cols[0], w_first, row_tile, col_tile, offset, width, nbins, n_off)
    inner_mask = band_mask(row_tile, col_tile, -4, inner_size, width, nbins, n_off)
    hidden = jnp.where(
        inner_mask[:, None, :], jnp.maximum(pre + b_first[None, :, None], 0.0), 0.0
    )
    result = second_conv(hidden.astype(jnp.bfloat16), w_second, b_second)
    return result[None, None, None]


def solution(mesh):
    placed = (P("diag", None, None, None), P(), P(), P(), P())
    return jax.shard_map(
        local,
        mesh=mesh,
        in_specs=placed,
        out_specs=P("diag", "off", None, None, None, None),
        check_vma=False,
    )
```

```python
import jax
import jax.numpy as jnp
from jax import lax
from jax.sharding import PartitionSpec as P
from jax.experimental import pallas as pl


def band_mask(row_tile, col_tile, start, extent, width, nbins, offsets_total):
    offsets = start + jnp.arange(extent, dtype=jnp.int32)
    row_bins = row_tile * width + offsets
    col_bins = col_tile * width + offsets
    row_ok = (row_bins >= 0) & (row_bins < nbins)
    col_ok = (col_bins >= 0) & (col_bins < nbins)
    gap = jnp.floor_divide(col_bins, width)[None, :] - jnp.floor_divide(row_bins, width)[:, None]
    return row_ok[:, None] & col_ok[None, :] & (gap >= 0) & (gap < offsets_total)


def fetch(trunk, shift_of, n_diag, n_off, offset):
    pairs = []
    for d in range(n_diag):
        for o in range(n_off):
            src = d + shift_of(o)
            if 0 <= src < n_diag and src != d:
                pairs.append((src * n_off + o, d * n_off + o))
    moved = lax.ppermute(trunk, ("diag", "off"), pairs)
    selves = [o for o in range(n_off) if shift_of(o) == 0]
    if not selves:
        return moved
    is_self = jnp.zeros((), jnp.bool_)
    for o in selves:
        is_self = is_self | (offset == o)
    return jnp.where(is_self, trunk, moved)


def block_indicator(tile, start, extent, width, nbins):
    bins = tile * width + start + jnp.arange(extent, dtype=jnp.int32)
    ok = (bins >= 0) & (bins < nbins)
    block = jnp.floor_divide(bins, width) - tile + 1
    return (ok[None, :] & (block[None, :] == jnp.arange(3, dtype=jnp.int32)[:, None])).astype(jnp.float32)


def split_bf16(value):
    high = lax.reduce_precision(value, exponent_bits=8, mantissa_bits=7)
    low = value - high
    return high.astype(jnp.bfloat16), low.astype(jnp.bfloat16)


def first_conv(rows, cols, w_first, row_tile, col_tile, offset, width, nbins, n_off):
    channels = rows.shape[0]
    extent = rows.shape[1]
    size = extent - 4
    a_ind = block_indicator(row_tile, -6, extent, width, nbins)
    b_ind = block_indicator(col_tile, -6, extent, width, nbins)
    steps = jnp.arange(3, dtype=jnp.int32)
    gap = offset + steps[None, :] - steps[:, None]
    g = ((gap >= 0) & (gap < n_off)).astype(jnp.float32)
    r = jnp.einsum("hcuv,ci->uvhi", w_first[:, :channels], rows, preferred_element_type=jnp.float32)
    c = jnp.einsum("hcuv,cj->uvhj", w_first[:, channels:], cols, preferred_element_type=jnp.float32)
    p_row = sum(
        a_ind[None, None, :, 2 * u : 2 * u + size] * r[u][:, :, None, 2 * u : 2 * u + size]
        for u in range(3)
    )
    b_sel = jnp.einsum("ab,bj->aj", g, b_ind)
    q_col = jnp.stack([b_sel[:, 2 * v : 2 * v + size] for v in range(3)], axis=1)
    p_col = sum(
        b_ind[None, None, :, 2 * v : 2 * v + size] * c[:, v][:, :, None, 2 * v : 2 * v + size]
        for v in range(3)
    )
    a_sel = jnp.einsum("ab,ai->bi", g, a_ind)
    q_row = jnp.stack([a_sel[:, 2 * u : 2 * u + size] for u in range(3)], axis=1)
    taps = 9
    hid = p_row.shape[1]
    p_row = jnp.transpose(p_row, (3, 1, 2, 0)).reshape(size, hid, taps)
    p_col = jnp.transpose(p_col, (2, 0, 1, 3)).reshape(taps, hid, size)
    p_row_hi, p_row_lo = split_bf16(p_row)
    p_col_hi, p_col_lo = split_bf16(p_col)
    q_col = q_col.reshape(taps, size).astype(jnp.bfloat16)
    q_row = jnp.transpose(q_row, (2, 0, 1)).reshape(size, taps).astype(jnp.bfloat16)
    p_row_both = jnp.concatenate([p_row_hi, p_row_lo], axis=2)
    p_col_both = jnp.concatenate([p_col_hi, p_col_lo], axis=0)
    term_row = jnp.einsum("ihk,kj->ihj", p_row_both, jnp.concatenate([q_col, q_col], axis=0),
                          preferred_element_type=jnp.float32)
    term_col = jnp.einsum("ik,khj->ihj", jnp.concatenate([q_row, q_row], axis=1), p_col_both,
                          preferred_element_type=jnp.float32)
    return term_row + term_col


ROWS_PER_STEP = 8


def second_conv_kernel(w_ref, b_ref, hidden_ref, out_ref):
    step = pl.program_id(0)
    width = out_ref.shape[2]
    for r in range(ROWS_PER_STEP):
        i = step * ROWS_PER_STEP + r
        acc = None
        for u in range(3):
            row = hidden_ref[i + 4 * u]
            for v in range(3):
                part = jnp.dot(w_ref[3 * u + v], row[:, 4 * v : 4 * v + width],
                               preferred_element_type=jnp.float32)
                acc = part if acc is None else acc + part
        out_ref[:, r, :] = (acc + b_ref[...]).astype(out_ref.dtype)


def second_conv(hidden, w_second, b_second):
    rows_in, hid, cols_in = hidden.shape
    width = rows_in - 8
    taps = jnp.transpose(w_second, (2, 3, 0, 1)).reshape(9, hid, hid)
    return pl.pallas_call(
        second_conv_kernel,
        grid=(width // ROWS_PER_STEP,),
        in_specs=[
            pl.BlockSpec((9, hid, hid), lambda s: (0, 0, 0)),
            pl.BlockSpec((hid, 1), lambda s: (0, 0)),
            pl.BlockSpec((rows_in, hid, cols_in), lambda s: (0, 0, 0)),
        ],
        out_specs=pl.BlockSpec((hid, ROWS_PER_STEP, width), lambda s: (0, s, 0)),
        out_shape=jax.ShapeDtypeStruct((hid, width, width), jnp.bfloat16),
    )(taps, b_second.reshape(hid, 1), hidden)


def local(trunk, w_first, b_first, w_second, b_second):
    samples = trunk.shape[1]
    channels = trunk.shape[2]
    width = trunk.shape[3]
    hidden_width = w_first.shape[0]
    n_off = lax.axis_size("off")
    n_diag = lax.axis_size("diag")
    nbins = n_diag * width
    row_tile = lax.axis_index("diag")
    offset = lax.axis_index("off")
    col_tile = row_tile + offset

    row_prev = fetch(trunk, lambda o: -1, n_diag, n_off, offset)
    row_next = fetch(trunk, lambda o: 1, n_diag, n_off, offset)
    row_after = fetch(trunk, lambda o: 2, n_diag, n_off, offset)
    line = jnp.concatenate([row_prev, trunk, row_next, row_after], axis=0)
    pairs = [
        ((d + o - 1) * n_off + o, d * n_off + o)
        for d in range(n_diag)
        for o in range(2, n_off)
        if d + o - 1 < n_diag
    ]
    moved = lax.ppermute(line, ("diag", "off"), pairs)
    col_panels = jnp.where(offset == 0, line[0:3], jnp.where(offset == 1, line[1:4], moved[1:4]))

    row_line = jnp.concatenate([line[0], line[1], line[2]], axis=-1)
    col_line = jnp.concatenate([col_panels[0], col_panels[1], col_panels[2]], axis=-1)

    extent = width + 12
    inner_size = width + 8
    rows = row_line[:, :, width - 6 : width - 6 + extent]
    cols = col_line[:, :, width - 6 : width - 6 + extent]
    pre = first_conv(rows[0], cols[0], w_first, row_tile, col_tile, offset, width, nbins, n_off)
    inner_mask = band_mask(row_tile, col_tile, -4, inner_size, width, nbins, n_off)
    hidden = jnp.where(
        inner_mask[:, None, :], jnp.maximum(pre + b_first[None, :, None], 0.0), 0.0
    )
    result = second_conv(hidden.astype(jnp.bfloat16), w_second, b_second)
    return result[None, None, None]


def solution(mesh):
    placed = (P("diag", None, None, None), P(), P(), P(), P())
    return jax.shard_map(
        local,
        mesh=mesh,
        in_specs=placed,
        out_specs=P("diag", "off", None, None, None, None),
        check_vma=False,
    )
```

```python
import jax
import jax.numpy as jnp
from jax import lax
from jax.sharding import PartitionSpec as P
from jax.experimental import pallas as pl


def band_mask(row_tile, col_tile, start, extent, width, nbins, offsets_total):
    offsets = start + jnp.arange(extent, dtype=jnp.int32)
    row_bins = row_tile * width + offsets
    col_bins = col_tile * width + offsets
    row_ok = (row_bins >= 0) & (row_bins < nbins)
    col_ok = (col_bins >= 0) & (col_bins < nbins)
    gap = jnp.floor_divide(col_bins, width)[None, :] - jnp.floor_divide(row_bins, width)[:, None]
    return row_ok[:, None] & col_ok[None, :] & (gap >= 0) & (gap < offsets_total)


def fetch(trunk, shift_of, n_diag, n_off, offset):
    pairs = []
    for d in range(n_diag):
        for o in range(n_off):
            src = d + shift_of(o)
            if 0 <= src < n_diag and src != d:
                pairs.append((src * n_off + o, d * n_off + o))
    moved = lax.ppermute(trunk, ("diag", "off"), pairs)
    selves = [o for o in range(n_off) if shift_of(o) == 0]
    if not selves:
        return moved
    is_self = jnp.zeros((), jnp.bool_)
    for o in selves:
        is_self = is_self | (offset == o)
    return jnp.where(is_self, trunk, moved)


def block_indicator(tile, start, extent, width, nbins):
    bins = tile * width + start + jnp.arange(extent, dtype=jnp.int32)
    ok = (bins >= 0) & (bins < nbins)
    block = jnp.floor_divide(bins, width) - tile + 1
    return (ok[None, :] & (block[None, :] == jnp.arange(3, dtype=jnp.int32)[:, None])).astype(jnp.float32)


def split_bf16(value):
    high = lax.reduce_precision(value, exponent_bits=8, mantissa_bits=7)
    low = value - high
    return high.astype(jnp.bfloat16), low.astype(jnp.bfloat16)


def first_conv(rows, cols, w_first, row_tile, col_tile, offset, width, nbins, n_off):
    channels = rows.shape[0]
    extent = rows.shape[1]
    size = extent - 4
    a_ind = block_indicator(row_tile, -6, extent, width, nbins)
    b_ind = block_indicator(col_tile, -6, extent, width, nbins)
    steps = jnp.arange(3, dtype=jnp.int32)
    gap = offset + steps[None, :] - steps[:, None]
    g = ((gap >= 0) & (gap < n_off)).astype(jnp.float32)
    r = jnp.einsum("hcuv,ci->uvhi", w_first[:, :channels], rows, preferred_element_type=jnp.float32)
    c = jnp.einsum("hcuv,cj->uvhj", w_first[:, channels:], cols, preferred_element_type=jnp.float32)
    p_row = sum(
        a_ind[None, None, :, 2 * u : 2 * u + size] * r[u][:, :, None, 2 * u : 2 * u + size]
        for u in range(3)
    )
    b_sel = jnp.einsum("ab,bj->aj", g, b_ind)
    q_col = jnp.stack([b_sel[:, 2 * v : 2 * v + size] for v in range(3)], axis=1)
    p_col = sum(
        b_ind[None, None, :, 2 * v : 2 * v + size] * c[:, v][:, :, None, 2 * v : 2 * v + size]
        for v in range(3)
    )
    a_sel = jnp.einsum("ab,ai->bi", g, a_ind)
    q_row = jnp.stack([a_sel[:, 2 * u : 2 * u + size] for u in range(3)], axis=1)
    taps = 9
    hid = p_row.shape[1]
    p_row = jnp.transpose(p_row, (3, 1, 2, 0)).reshape(size, hid, taps)
    p_col = jnp.transpose(p_col, (2, 0, 1, 3)).reshape(taps, hid, size)
    p_row_hi, p_row_lo = split_bf16(p_row)
    p_col_hi, p_col_lo = split_bf16(p_col)
    q_col = q_col.reshape(taps, size).astype(jnp.bfloat16)
    q_row = jnp.transpose(q_row, (2, 0, 1)).reshape(size, taps).astype(jnp.bfloat16)
    p_row_both = jnp.concatenate([p_row_hi, p_row_lo], axis=2)
    p_col_both = jnp.concatenate([p_col_hi, p_col_lo], axis=0)
    term_row = jnp.einsum("ihk,kj->ihj", p_row_both, jnp.concatenate([q_col, q_col], axis=0),
                          preferred_element_type=jnp.float32)
    term_col = jnp.einsum("ik,khj->ihj", jnp.concatenate([q_row, q_row], axis=1), p_col_both,
                          preferred_element_type=jnp.float32)
    return term_row + term_col


ROWS_PER_STEP = 16


def second_conv_kernel(w_ref, b_ref, hidden_ref, out_ref):
    step = pl.program_id(0)
    width = out_ref.shape[2]
    for r in range(ROWS_PER_STEP):
        i = step * ROWS_PER_STEP + r
        acc = None
        for u in range(3):
            row = hidden_ref[i + 4 * u]
            for v in range(3):
                part = jnp.dot(w_ref[3 * u + v], row[:, 4 * v : 4 * v + width],
                               preferred_element_type=jnp.float32)
                acc = part if acc is None else acc + part
        out_ref[:, r, :] = (acc + b_ref[...]).astype(out_ref.dtype)


def second_conv(hidden, w_second, b_second):
    rows_in, hid, cols_in = hidden.shape
    width = rows_in - 8
    taps = jnp.transpose(w_second, (2, 3, 0, 1)).reshape(9, hid, hid)
    return pl.pallas_call(
        second_conv_kernel,
        grid=(width // ROWS_PER_STEP,),
        in_specs=[
            pl.BlockSpec((9, hid, hid), lambda s: (0, 0, 0)),
            pl.BlockSpec((hid, 1), lambda s: (0, 0)),
            pl.BlockSpec((rows_in, hid, cols_in), lambda s: (0, 0, 0)),
        ],
        out_specs=pl.BlockSpec((hid, ROWS_PER_STEP, width), lambda s: (0, s, 0)),
        out_shape=jax.ShapeDtypeStruct((hid, width, width), jnp.bfloat16),
    )(taps, b_second.reshape(hid, 1), hidden)


def local(trunk, w_first, b_first, w_second, b_second):
    samples = trunk.shape[1]
    channels = trunk.shape[2]
    width = trunk.shape[3]
    hidden_width = w_first.shape[0]
    n_off = lax.axis_size("off")
    n_diag = lax.axis_size("diag")
    nbins = n_diag * width
    row_tile = lax.axis_index("diag")
    offset = lax.axis_index("off")
    col_tile = row_tile + offset

    row_prev = fetch(trunk, lambda o: -1, n_diag, n_off, offset)
    row_next = fetch(trunk, lambda o: 1, n_diag, n_off, offset)
    col_prev = fetch(trunk, lambda o: o - 1, n_diag, n_off, offset)
    col_here = fetch(trunk, lambda o: o, n_diag, n_off, offset)
    col_next = fetch(trunk, lambda o: o + 1, n_diag, n_off, offset)

    row_line = jnp.concatenate([row_prev[0], trunk[0], row_next[0]], axis=-1)
    col_line = jnp.concatenate([col_prev[0], col_here[0], col_next[0]], axis=-1)

    extent = width + 12
    inner_size = width + 8
    rows = row_line[:, :, width - 6 : width - 6 + extent]
    cols = col_line[:, :, width - 6 : width - 6 + extent]
    pre = first_conv(rows[0], cols[0], w_first, row_tile, col_tile, offset, width, nbins, n_off)
    inner_mask = band_mask(row_tile, col_tile, -4, inner_size, width, nbins, n_off)
    hidden = jnp.where(
        inner_mask[:, None, :], jnp.maximum(pre + b_first[None, :, None], 0.0), 0.0
    )
    result = second_conv(hidden.astype(jnp.bfloat16), w_second, b_second)
    return result[None, None, None]


def solution(mesh):
    placed = (P("diag", None, None, None), P(), P(), P(), P())
    return jax.shard_map(
        local,
        mesh=mesh,
        in_specs=placed,
        out_specs=P("diag", "off", None, None, None, None),
        check_vma=False,
    )
```

```python
import jax
import jax.numpy as jnp
from jax import lax
from jax.sharding import PartitionSpec as P
from jax.experimental import pallas as pl


def band_mask(row_tile, col_tile, start, extent, width, nbins, offsets_total):
    offsets = start + jnp.arange(extent, dtype=jnp.int32)
    row_bins = row_tile * width + offsets
    col_bins = col_tile * width + offsets
    row_ok = (row_bins >= 0) & (row_bins < nbins)
    col_ok = (col_bins >= 0) & (col_bins < nbins)
    gap = jnp.floor_divide(col_bins, width)[None, :] - jnp.floor_divide(row_bins, width)[:, None]
    return row_ok[:, None] & col_ok[None, :] & (gap >= 0) & (gap < offsets_total)


def fetch(trunk, shift_of, n_diag, n_off, offset):
    pairs = []
    for d in range(n_diag):
        for o in range(n_off):
            src = d + shift_of(o)
            if 0 <= src < n_diag and src != d:
                pairs.append((src * n_off + o, d * n_off + o))
    moved = lax.ppermute(trunk, ("diag", "off"), pairs)
    selves = [o for o in range(n_off) if shift_of(o) == 0]
    if not selves:
        return moved
    is_self = jnp.zeros((), jnp.bool_)
    for o in selves:
        is_self = is_self | (offset == o)
    return jnp.where(is_self, trunk, moved)


def block_indicator(tile, start, extent, width, nbins):
    bins = tile * width + start + jnp.arange(extent, dtype=jnp.int32)
    ok = (bins >= 0) & (bins < nbins)
    block = jnp.floor_divide(bins, width) - tile + 1
    return (ok[None, :] & (block[None, :] == jnp.arange(3, dtype=jnp.int32)[:, None])).astype(jnp.float32)


def split_bf16(value):
    high = lax.reduce_precision(value, exponent_bits=8, mantissa_bits=7)
    low = value - high
    return high.astype(jnp.bfloat16), low.astype(jnp.bfloat16)


def first_conv(rows, cols, w_first, row_tile, col_tile, offset, width, nbins, n_off):
    channels = rows.shape[0]
    extent = rows.shape[1]
    size = extent - 4
    a_ind = block_indicator(row_tile, -6, extent, width, nbins)
    b_ind = block_indicator(col_tile, -6, extent, width, nbins)
    steps = jnp.arange(3, dtype=jnp.int32)
    gap = offset + steps[None, :] - steps[:, None]
    g = ((gap >= 0) & (gap < n_off)).astype(jnp.float32)
    r = jnp.einsum("hcuv,ci->uvhi", w_first[:, :channels], rows, preferred_element_type=jnp.float32)
    c = jnp.einsum("hcuv,cj->uvhj", w_first[:, channels:], cols, preferred_element_type=jnp.float32)
    p_row = sum(
        a_ind[None, None, :, 2 * u : 2 * u + size] * r[u][:, :, None, 2 * u : 2 * u + size]
        for u in range(3)
    )
    b_sel = jnp.einsum("ab,bj->aj", g, b_ind)
    q_col = jnp.stack([b_sel[:, 2 * v : 2 * v + size] for v in range(3)], axis=1)
    p_col = sum(
        b_ind[None, None, :, 2 * v : 2 * v + size] * c[:, v][:, :, None, 2 * v : 2 * v + size]
        for v in range(3)
    )
    a_sel = jnp.einsum("ab,ai->bi", g, a_ind)
    q_row = jnp.stack([a_sel[:, 2 * u : 2 * u + size] for u in range(3)], axis=1)
    taps = 9
    hid = p_row.shape[1]
    p_row = jnp.transpose(p_row, (3, 1, 2, 0)).reshape(size, hid, taps)
    p_col = jnp.transpose(p_col, (2, 0, 1, 3)).reshape(taps, hid, size)
    p_row_hi, p_row_lo = split_bf16(p_row)
    p_col_hi, p_col_lo = split_bf16(p_col)
    q_col = q_col.reshape(taps, size).astype(jnp.bfloat16)
    q_row = jnp.transpose(q_row, (2, 0, 1)).reshape(size, taps).astype(jnp.bfloat16)
    p_row_both = jnp.concatenate([p_row_hi, p_row_lo], axis=2)
    p_col_both = jnp.concatenate([p_col_hi, p_col_lo], axis=0)
    term_row = jnp.einsum("ihk,kj->ihj", p_row_both, jnp.concatenate([q_col, q_col], axis=0),
                          preferred_element_type=jnp.float32)
    term_col = jnp.einsum("ik,khj->ihj", jnp.concatenate([q_row, q_row], axis=1), p_col_both,
                          preferred_element_type=jnp.float32)
    return term_row + term_col


ROWS_PER_STEP = 32


def second_conv_kernel(w_ref, b_ref, hidden_ref, out_ref):
    step = pl.program_id(0)
    width = out_ref.shape[2]
    for r in range(ROWS_PER_STEP):
        i = step * ROWS_PER_STEP + r
        acc = None
        for u in range(3):
            row = hidden_ref[i + 4 * u]
            for v in range(3):
                part = jnp.dot(w_ref[3 * u + v], row[:, 4 * v : 4 * v + width],
                               preferred_element_type=jnp.float32)
                acc = part if acc is None else acc + part
        out_ref[:, r, :] = (acc + b_ref[...]).astype(out_ref.dtype)


def second_conv(hidden, w_second, b_second):
    rows_in, hid, cols_in = hidden.shape
    width = rows_in - 8
    taps = jnp.transpose(w_second, (2, 3, 0, 1)).reshape(9, hid, hid)
    return pl.pallas_call(
        second_conv_kernel,
        grid=(width // ROWS_PER_STEP,),
        in_specs=[
            pl.BlockSpec((9, hid, hid), lambda s: (0, 0, 0)),
            pl.BlockSpec((hid, 1), lambda s: (0, 0)),
            pl.BlockSpec((rows_in, hid, cols_in), lambda s: (0, 0, 0)),
        ],
        out_specs=pl.BlockSpec((hid, ROWS_PER_STEP, width), lambda s: (0, s, 0)),
        out_shape=jax.ShapeDtypeStruct((hid, width, width), jnp.bfloat16),
    )(taps, b_second.reshape(hid, 1), hidden)


def local(trunk, w_first, b_first, w_second, b_second):
    samples = trunk.shape[1]
    channels = trunk.shape[2]
    width = trunk.shape[3]
    hidden_width = w_first.shape[0]
    n_off = lax.axis_size("off")
    n_diag = lax.axis_size("diag")
    nbins = n_diag * width
    row_tile = lax.axis_index("diag")
    offset = lax.axis_index("off")
    col_tile = row_tile + offset

    row_prev = fetch(trunk, lambda o: -1, n_diag, n_off, offset)
    row_next = fetch(trunk, lambda o: 1, n_diag, n_off, offset)
    col_prev = fetch(trunk, lambda o: o - 1, n_diag, n_off, offset)
    col_here = fetch(trunk, lambda o: o, n_diag, n_off, offset)
    col_next = fetch(trunk, lambda o: o + 1, n_diag, n_off, offset)

    row_line = jnp.concatenate([row_prev[0], trunk[0], row_next[0]], axis=-1)
    col_line = jnp.concatenate([col_prev[0], col_here[0], col_next[0]], axis=-1)

    extent = width + 12
    inner_size = width + 8
    rows = row_line[:, :, width - 6 : width - 6 + extent]
    cols = col_line[:, :, width - 6 : width - 6 + extent]
    pre = first_conv(rows[0], cols[0], w_first, row_tile, col_tile, offset, width, nbins, n_off)
    inner_mask = band_mask(row_tile, col_tile, -4, inner_size, width, nbins, n_off)
    hidden = jnp.where(
        inner_mask[:, None, :], jnp.maximum(pre + b_first[None, :, None], 0.0), 0.0
    )
    result = second_conv(hidden.astype(jnp.bfloat16), w_second, b_second)
    return result[None, None, None]


def solution(mesh):
    placed = (P("diag", None, None, None), P(), P(), P(), P())
    return jax.shard_map(
        local,
        mesh=mesh,
        in_specs=placed,
        out_specs=P("diag", "off", None, None, None, None),
        check_vma=False,
    )
```
